128 devices in a mesh: src: 4 (over y_hi, core), gx: 4 (over x), yz: 8 (over z, y_lo).
Axes of the slice: x: 4, y: 4 (y_hi: 2, y_lo: 2; y = y_hi * 2 + y_lo), z: 4, core: 2. Of those that a mesh axis runs over, the one named last changes fastest.
Arguments:
- warm_start: float32 [2, 16, 128, 128, 256], P(None, 'src', 'gx', 'yz'), may hold values from -1 to 1, as said below
- conductivity: float32 [128, 128, 256], P('gx', 'yz'), may hold values from 0.2 to 5
- currents: float32 [16], P('src'), may hold values from 4 to 16
- electrodes: int32 [16, 2], P('src'), may hold values from 0 to 4194303
- receivers: int32 [256], replicated, may hold values from 0 to 4194303
- weights: float32 [16, 256], P('src'), may hold values from -24 to 24
Outputs:
- solutions: float32 [2, 16, 128, 128, 256], P(None, 'src', 'gx', 'yz')
- gradient: float32 [128, 128, 256], P('gx', 'yz', 'src')
The draws below stay inside these ranges and needn't reach their ends.
Inputs may be any that keep to these rules, and one draw needn't show every extreme that they name: `electrodes`: each entry is a linear cell index as in the reference program; two entries may name the same cell. `receivers`: each entry is a linear cell index as in the reference program; two entries may name the same cell. `warm_start`: previous potentials, finite.
All inputs are finite; a program needn't handle non-finite values.
Results may differ from the reference program's by a relative error of at most 0.0003.
Values sent between devices are 32-bit elements; how exact they have to be, the bound alone decides.
No kernel may reach another device: no remote copies, remote signals or barrier semaphores. Data moves between devices by JAX's collectives and lax.ppermute only.
A program may use at most 128 MiB of HBM per device.

```python
import math
import jax
import jax.numpy as jnp
from jax import lax

NSRC = 16
NREC = 256
ITERS = 2
SRC_GRP = 4
NX = 128
NY = 128
NZ = 256


def sine_profile(count, wave):
    position = (jnp.arange(count, dtype=jnp.float32) + 0.5) / count
    return jnp.sin(math.pi * wave * position)


def draw_warm_start(key, part):
    shape = (2, NSRC, NX, NY, NZ)
    amp_key = jax.random.fold_in(key, 11)
    noise_key = jax.random.fold_in(key, 23)
    waves = ((1, 1, 1), (2, 1, 2), (1, 2, 1))
    amplitudes = 0.05 * jnp.clip(jax.random.normal(amp_key, (3, 2, NSRC), jnp.float32), -3.0, 3.0)
    field = jnp.zeros(shape, jnp.float32)
    for number, wave in enumerate(waves):
        mode = sine_profile(NX, wave[0])[:, None, None] * sine_profile(NY, wave[1])[None, :, None] * sine_profile(NZ, wave[2])[None, None, :]
        field = field + amplitudes[number][:, :, None, None, None] * mode[None, None]
    noise = 0.0001 * jnp.clip(jax.random.normal(noise_key, shape, jnp.float32), -6.0, 6.0)
    return (field + noise).astype(jnp.float32)


def place_ends(entries, key, least, top_value):
    longest = entries.shape.index(max(entries.shape))
    spots = []
    for shift in (0, 1):
        where = [jax.random.randint(jax.random.fold_in(key, axis), (), 0, length) for axis, length in enumerate(entries.shape)]
        where[longest] = (where[longest] + shift) % entries.shape[longest]
        spots.append(tuple(where))
    return entries.at[spots[0]].set(least).at[spots[1]].set(top_value)


def block_scale(rng, extent, split, smallest, high):
    def one(dim, parts):
        heights = jax.random.uniform(jax.random.fold_in(jax.random.fold_in(rng, 6), dim), (parts,), jnp.float32, smallest / len(split), high / len(split))
        return jnp.repeat(jnp.exp(heights), extent[dim] // parts).reshape((-1,) + (1,) * (len(extent) - dim - 1))

    loudness = one(*split[0])
    for cut in split[1:]:
        loudness = loudness * one(*cut)
    return loudness


def gaussian(rng, dims, width, limit, pieces=(), kind=jnp.bfloat16):
    level = block_scale(rng, dims, pieces, -0.22, 0.18) if pieces else 1.0
    array = jax.random.normal(rng, dims, jnp.float32) * width * level
    return jnp.minimum(jnp.maximum(array, -limit), limit).astype(kind)


def setup_inputs(seed: int = 0) -> dict:
    key_of = jax.random.split(jax.random.key(seed), 7)
    warm_start = draw_warm_start(jax.random.fold_in(key_of[6], 71), 0)
    conductivity = jnp.clip(jnp.exp(math.log(5.0) - 3.218876 * jax.random.uniform(key_of[1], (NX, NY, NZ), jnp.float32) ** block_scale(key_of[1], (NX, NY, NZ), ((0, 4), (1, 8)), -0.2, 0.2)), 0.2, 5.0)
    currents = jnp.clip(jnp.exp(math.log(16.0) - 1.3862944 * jax.random.uniform(key_of[2], (NSRC,), jnp.float32) ** block_scale(key_of[2], (NSRC,), ((0, 4),), -0.2, 0.2)), 4.0, 16.0)
    electrodes = place_ends(jax.random.randint(key_of[3], (NSRC, 2), 0, NX * NY * NZ), jax.random.fold_in(key_of[3], 1), 0, (NX * NY * NZ) - 1).astype(jnp.int32)
    receivers = place_ends(jax.random.randint(key_of[4], (NREC,), 0, NX * NY * NZ), jax.random.fold_in(key_of[4], 1), 0, (NX * NY * NZ) - 1).astype(jnp.int32)
    weights = gaussian(key_of[5], (NSRC, NREC), 4.0, 24.0, ((0, 4),), jnp.float32)
    return dict(warm_start=warm_start, conductivity=conductivity, currents=currents, electrodes=electrodes, receivers=receivers, weights=weights)


highest = lax.Precision.HIGHEST

def neighbours(padded):
    middle = padded[..., 1:-1, 1:-1, :]
    zeros = jnp.zeros(middle.shape[:-1] + (1,), middle.dtype)
    return (padded[..., 2:, 1:-1, :], padded[..., :-2, 1:-1, :], padded[..., 1:-1, 2:, :], padded[..., 1:-1, :-2, :], jnp.concatenate([middle[..., 1:], zeros], axis=-1), jnp.concatenate([zeros, middle[..., :-1]], axis=-1))

def pad_plane(field):
    widths = [(0, 0)] * (field.ndim - 3) + [(1, 1), (1, 1), (0, 0)]
    return jnp.pad(field, widths)

def apply(padded, faces, diagonal):
    field = padded[..., 1:-1, 1:-1, :]
    total = diagonal * field
    for weight, near in zip(faces, neighbours(padded)):
        total = total - weight * near
    return total

def gram(left, right):
    return jnp.einsum('axyz,bxyz->ab', left, right, precision=highest)

def combine(coef, field):
    return jnp.einsum('ab,axyz->bxyz', coef, field, precision=highest)

def solve_small(matrix, rhs):
    factor = jnp.linalg.cholesky(matrix)
    middle = lax.linalg.triangular_solve(factor, rhs, left_side=True, lower=True)
    return lax.linalg.triangular_solve(factor, middle, left_side=True, lower=True, transpose_a=True)

def local_gradient(padded_solution, count):
    field = padded_solution[:, 1:-1, 1:-1, :]
    forward = field[:count]
    adjoint = field[count:]
    total = jnp.zeros(field.shape[1:], jnp.float32)
    for near_fwd, near_adj in zip(neighbours(padded_solution[:count]), neighbours(padded_solution[count:])):
        total = total + jnp.sum((forward - near_fwd) * (adjoint - near_adj), axis=0)
    return -0.5 * total

def reference(warm_start, conductivity, currents, electrodes, receivers, weights):
    faces = tuple((0.5 * (conductivity + near) for near in neighbours(pad_plane(conductivity))))
    diagonal = faces[0]
    for weight in faces[1:]:
        diagonal = diagonal + weight

    def solve_group(group):
        start = (group * SRC_GRP).astype(jnp.int32)
        rows = start + jnp.arange(SRC_GRP, dtype=jnp.int32)
        local = jnp.arange(SRC_GRP, dtype=jnp.int32)
        field = jnp.zeros((2, SRC_GRP, NX * NY * NZ), jnp.float32)
        field = field.at[0, local, electrodes[rows, 0]].add(currents[rows])
        field = field.at[0, local, electrodes[rows, 1]].add(-currents[rows])
        field = field.at[1, local[:, None], receivers[None, :]].add(weights[rows])
        rhs = field.reshape(2 * SRC_GRP, NX, NY, NZ)
        solution = lax.dynamic_slice_in_dim(warm_start, start, SRC_GRP, 1).reshape(2 * SRC_GRP, NX, NY, NZ)
        residual = rhs - apply(pad_plane(solution), faces, diagonal)
        precond = residual / diagonal
        direction = precond
        inner = gram(residual, precond)
        for step in range(ITERS):
            image = apply(pad_plane(direction), faces, diagonal)
            curve = gram(direction, image)
            alpha = solve_small(curve, inner)
            solution = solution + combine(alpha, direction)
            residual = residual - combine(alpha, image)
            if step + 1 < ITERS:
                precond = residual / diagonal
                fresh = gram(residual, precond)
                beta = solve_small(inner, fresh)
                direction = precond + combine(beta, direction)
                inner = fresh
        return solution
    solved = lax.map(solve_group, jnp.arange(NSRC // SRC_GRP, dtype=jnp.int32))

    def accumulate(total, solution):
        return (total + local_gradient(pad_plane(solution), SRC_GRP), None)
    gradient, unused = lax.scan(accumulate, jnp.zeros((NX, NY, NZ), jnp.float32), solved)
    grouped = solved.reshape(NSRC // SRC_GRP, 2, SRC_GRP, NX, NY, NZ)
    solutions = jnp.moveaxis(grouped, 0, 1).reshape(2, NSRC, NX, NY, NZ)
    return (solutions, gradient)
```

```python
import jax
import jax.numpy as jnp
from jax import lax
from jax.sharding import PartitionSpec as P

ITERS = 2


highest = lax.Precision.HIGHEST


def with_halo(shard, sides, width):
    for axis, dim in sides:
        count, length = (lax.axis_size(axis), shard.shape[dim])
        up = [(i, (i + 1) % count) for i in range(count - 1)]
        down = [(j, i) for i, j in up]
        last = lax.slice_in_dim(shard, length - width, length, axis=dim)
        initial = lax.slice_in_dim(shard, 0, width, axis=dim)
        before = lax.ppermute(last, axis, up)
        after = lax.ppermute(initial, axis, down)
        shard = jnp.concatenate([before, shard, after], axis=dim)
    return shard


def neighbours(padded):
    middle = padded[..., 1:-1, 1:-1, :]
    zeros = jnp.zeros(middle.shape[:-1] + (1,), middle.dtype)
    return (
        padded[..., 2:, 1:-1, :],
        padded[..., :-2, 1:-1, :],
        padded[..., 1:-1, 2:, :],
        padded[..., 1:-1, :-2, :],
        jnp.concatenate([middle[..., 1:], zeros], axis=-1),
        jnp.concatenate([zeros, middle[..., :-1]], axis=-1),
    )


def apply(padded, faces, diagonal):
    field = padded[..., 1:-1, 1:-1, :]
    total = diagonal * field
    for weight, near in zip(faces, neighbours(padded)):
        total = total - weight * near
    return total


def gram(left, right):
    return jnp.einsum("axyz,bxyz->ab", left, right, precision=highest)


def combine(coef, field):
    return jnp.einsum("ab,axyz->bxyz", coef, field, precision=highest)


def solve_small(matrix, rhs):
    factor = jnp.linalg.cholesky(matrix)
    middle = lax.linalg.triangular_solve(factor, rhs, left_side=True, lower=True)
    return lax.linalg.triangular_solve(factor, middle, left_side=True, lower=True, transpose_a=True)


def extend(field):
    return with_halo(field, (("gx", 1), ("yz", 2)), 1)


def shifted_sum(value, axis, stride, count):
    size = lax.axis_size(axis)
    total = value
    for step in range(1, count):
        pairs = [(i, (i + stride * step) % size) for i in range(size)]
        total = total + lax.ppermute(value, axis, pairs)
    return total


def reduce_grid(value):
    value = shifted_sum(value, "gx", 1, lax.axis_size("gx"))
    size = lax.axis_size("yz")
    value = value + lax.ppermute(value, "yz", [(i, i ^ 1) for i in range(size)])
    return shifted_sum(value, "yz", 2, size // 2)


def global_gram(left, right):
    return reduce_grid(gram(left, right))


def scatter_sources(partial_value):
    size = lax.axis_size("src")
    width = partial_value.shape[2] // size
    index = lax.axis_index("src")

    def chunk(offset):
        return lax.dynamic_slice_in_dim(partial_value, ((index + offset) % size) * width, width, axis=2)

    total = chunk(0)
    for step in range(1, size):
        pairs = [(i, (i + step) % size) for i in range(size)]
        total = total + lax.ppermute(chunk(step), "src", pairs)
    return total


def local_sources(count, cells, currents, electrodes, receivers, weights):
    size_x, size_y, size_z = cells
    span_y = size_y * lax.axis_size("yz")
    anchor_x = lax.axis_index("gx") * size_x
    anchor_y = lax.axis_index("yz") * size_y

    def place(index):
        plane = span_y * size_z
        glob_x = index // plane
        glob_y = index % plane // size_z
        glob_z = index % size_z
        loc_x = glob_x - anchor_x
        loc_y = glob_y - anchor_y
        inside = (loc_x >= 0) & (loc_x < size_x) & (loc_y >= 0) & (loc_y < size_y)
        return jnp.where(
            inside, (loc_x * size_y + loc_y) * size_z + glob_z, size_x * size_y * size_z
        )

    local = jnp.arange(count, dtype=jnp.int32)
    field = jnp.zeros((2, count, size_x * size_y * size_z), jnp.float32)
    field = field.at[0, local, place(electrodes[:, 0])].add(currents, mode="drop")
    field = field.at[0, local, place(electrodes[:, 1])].add(-currents, mode="drop")
    field = field.at[1, local[:, None], place(receivers)[None, :]].add(weights, mode="drop")
    return field.reshape((2 * count,) + cells)


def on_device(warm_start, conductivity, currents, electrodes, receivers, weights):
    count = warm_start.shape[1]
    cells = warm_start.shape[2:]
    padded_cond = with_halo(conductivity, (("gx", 0), ("yz", 1)), 1)
    faces = tuple((0.5 * (conductivity + near) for near in neighbours(padded_cond)))
    diagonal = faces[0]
    for weight in faces[1:]:
        diagonal = diagonal + weight
    rhs = local_sources(count, cells, currents, electrodes, receivers, weights)
    solution = warm_start.reshape((2 * count,) + cells)
    padded_solution = extend(solution)
    residual = rhs - apply(padded_solution, faces, diagonal)
    precond = residual / diagonal
    direction = precond
    inner = gram(residual, precond)
    for step in range(ITERS):
        padded_direction = extend(direction)
        image = apply(padded_direction, faces, diagonal)
        if step == 0:
            inner, curve = reduce_grid(jnp.stack([inner, gram(direction, image)]))
        else:
            curve = global_gram(direction, image)
        alpha = solve_small(curve, inner)
        solution = solution + combine(alpha, direction)
        residual = residual - combine(alpha, image)
        if step + 1 < ITERS:
            precond = residual / diagonal
            fresh = global_gram(residual, precond)
            beta = solve_small(inner, fresh)
            direction = precond + combine(beta, direction)
            inner = fresh
    padded_solution = with_halo(solution, (("gx", 1), ("yz", 2)), 1)
    forward = solution[:count]
    adjoint = solution[count:]
    total = jnp.zeros(cells, jnp.float32)
    for near_fwd, near_adj in zip(
        neighbours(padded_solution[:count]), neighbours(padded_solution[count:])
    ):
        total = total + jnp.sum((forward - near_fwd) * (adjoint - near_adj), axis=0)
    partial_value = -0.5 * total
    gradient = scatter_sources(partial_value)
    return (solution.reshape(warm_start.shape), gradient)


def solution(mesh):
    return jax.shard_map(
        on_device,
        mesh=mesh,
        in_specs=(
            P(None, "src", "gx", "yz", None),
            P("gx", "yz", None),
            P("src"),
            P("src", None),
            P(),
            P("src", None),
        ),
        out_specs=(P(None, "src", "gx", "yz", None), P("gx", "yz", "src")),
        check_vma=False,
    )
```

```python
import jax
import jax.numpy as jnp
from jax import lax
from jax.sharding import PartitionSpec as P

ITERS = 2


highest = lax.Precision.HIGHEST


def with_halo(shard, sides, width):
    for axis, dim in sides:
        count, length = (lax.axis_size(axis), shard.shape[dim])
        up = [(i, (i + 1) % count) for i in range(count - 1)]
        down = [(j, i) for i, j in up]
        last = lax.slice_in_dim(shard, length - width, length, axis=dim)
        initial = lax.slice_in_dim(shard, 0, width, axis=dim)
        before = lax.ppermute(last, axis, up)
        after = lax.ppermute(initial, axis, down)
        shard = jnp.concatenate([before, shard, after], axis=dim)
    return shard


def neighbours(padded):
    middle = padded[..., 1:-1, 1:-1, :]
    zeros = jnp.zeros(middle.shape[:-1] + (1,), middle.dtype)
    return (
        padded[..., 2:, 1:-1, :],
        padded[..., :-2, 1:-1, :],
        padded[..., 1:-1, 2:, :],
        padded[..., 1:-1, :-2, :],
        jnp.concatenate([middle[..., 1:], zeros], axis=-1),
        jnp.concatenate([zeros, middle[..., :-1]], axis=-1),
    )


def apply(padded, faces, diagonal):
    field = padded[..., 1:-1, 1:-1, :]
    total = diagonal * field
    for weight, near in zip(faces, neighbours(padded)):
        total = total - weight * near
    return total


def gram(left, right):
    return jnp.einsum("axyz,bxyz->ab", left, right, precision=highest)


def combine(coef, field):
    return jnp.einsum("ab,axyz->bxyz", coef, field, precision=highest)


def solve_small(matrix, rhs):
    factor = jnp.linalg.cholesky(matrix)
    middle = lax.linalg.triangular_solve(factor, rhs, left_side=True, lower=True)
    return lax.linalg.triangular_solve(factor, middle, left_side=True, lower=True, transpose_a=True)


def extend(field):
    return with_halo(field, (("gx", 1), ("yz", 2)), 1)


def shifted_sum(value, axis, stride, count):
    size = lax.axis_size(axis)
    total = value
    for step in range(1, count):
        pairs = [(i, (i + stride * step) % size) for i in range(size)]
        total = total + lax.ppermute(value, axis, pairs)
    return total


def reduce_grid(value):
    value = shifted_sum(value, "gx", 1, lax.axis_size("gx"))
    size = lax.axis_size("yz")
    value = value + lax.ppermute(value, "yz", [(i, i ^ 1) for i in range(size)])
    return shifted_sum(value, "yz", 2, size // 2)


def global_gram(left, right):
    return reduce_grid(gram(left, right))


def scatter_sources(partial_value):
    size = lax.axis_size("src")
    width = partial_value.shape[2] // size
    index = lax.axis_index("src")

    def chunk(offset):
        return lax.dynamic_slice_in_dim(partial_value, ((index + offset) % size) * width, width, axis=2)

    total = chunk(0)
    for step in range(1, size):
        pairs = [(i, (i + step) % size) for i in range(size)]
        total = total + lax.ppermute(chunk(step), "src", pairs)
    return total


def local_sources(count, cells, currents, electrodes, receivers, weights):
    size_x, size_y, size_z = cells
    span_y = size_y * lax.axis_size("yz")
    anchor_x = lax.axis_index("gx") * size_x
    anchor_y = lax.axis_index("yz") * size_y

    def place(index):
        plane = span_y * size_z
        glob_x = index // plane
        glob_y = index % plane // size_z
        glob_z = index % size_z
        loc_x = glob_x - anchor_x
        loc_y = glob_y - anchor_y
        inside = (loc_x >= 0) & (loc_x < size_x) & (loc_y >= 0) & (loc_y < size_y)
        return jnp.where(
            inside, (loc_x * size_y + loc_y) * size_z + glob_z, size_x * size_y * size_z
        )

    local = jnp.arange(count, dtype=jnp.int32)
    field = jnp.zeros((2, count, size_x * size_y * size_z), jnp.float32)
    field = field.at[0, local, place(electrodes[:, 0])].add(currents, mode="drop")
    field = field.at[0, local, place(electrodes[:, 1])].add(-currents, mode="drop")
    field = field.at[1, local[:, None], place(receivers)[None, :]].add(weights, mode="drop")
    return field.reshape((2 * count,) + cells)


def on_device(warm_start, conductivity, currents, electrodes, receivers, weights):
    count = warm_start.shape[1]
    cells = warm_start.shape[2:]
    padded_cond = with_halo(conductivity, (("gx", 0), ("yz", 1)), 1)
    faces = tuple((0.5 * (conductivity + near) for near in neighbours(padded_cond)))
    diagonal = faces[0]
    for weight in faces[1:]:
        diagonal = diagonal + weight
    rhs = local_sources(count, cells, currents, electrodes, receivers, weights)
    solution = warm_start.reshape((2 * count,) + cells)
    padded_solution = extend(solution)
    residual = rhs - apply(padded_solution, faces, diagonal)
    precond = residual / diagonal
    direction = precond
    inner = gram(residual, precond)
    padded_direction = extend(direction)
    image = apply(padded_direction, faces, diagonal)
    inner, curve = reduce_grid(jnp.stack([inner, gram(direction, image)]))
    for step in range(ITERS):
        alpha = solve_small(curve, inner)
        solution = solution + combine(alpha, direction)
        if step + 1 < ITERS:
            residual = residual - combine(alpha, image)
            precond = residual / diagonal
            precond_image = apply(extend(precond), faces, diagonal)
            fresh, self_curve, cross = reduce_grid(jnp.stack(
                [gram(residual, precond), gram(precond, precond_image), gram(precond, image)]))
            beta = solve_small(inner, fresh)
            mixed = jnp.matmul(cross, beta, precision=highest)
            curve = (self_curve + mixed + mixed.T
                     + jnp.matmul(beta.T, jnp.matmul(curve, beta, precision=highest), precision=highest))
            direction = precond + combine(beta, direction)
            image = precond_image + combine(beta, image)
            inner = fresh
    padded_solution = with_halo(solution, (("gx", 1), ("yz", 2)), 1)
    forward = solution[:count]
    adjoint = solution[count:]
    total = jnp.zeros(cells, jnp.float32)
    for near_fwd, near_adj in zip(
        neighbours(padded_solution[:count]), neighbours(padded_solution[count:])
    ):
        total = total + jnp.sum((forward - near_fwd) * (adjoint - near_adj), axis=0)
    partial_value = -0.5 * total
    gradient = scatter_sources(partial_value)
    return (solution.reshape(warm_start.shape), gradient)


def solution(mesh):
    return jax.shard_map(
        on_device,
        mesh=mesh,
        in_specs=(
            P(None, "src", "gx", "yz", None),
            P("gx", "yz", None),
            P("src"),
            P("src", None),
            P(),
            P("src", None),
        ),
        out_specs=(P(None, "src", "gx", "yz", None), P("gx", "yz", "src")),
        check_vma=False,
    )
```

```python
import jax
import jax.numpy as jnp
from jax import lax
from jax.sharding import PartitionSpec as P

ITERS = 2


highest = lax.Precision.HIGHEST


def with_halo(shard, sides, width):
    for axis, dim in sides:
        count, length = (lax.axis_size(axis), shard.shape[dim])
        up = [(i, (i + 1) % count) for i in range(count - 1)]
        down = [(j, i) for i, j in up]
        last = lax.slice_in_dim(shard, length - width, length, axis=dim)
        initial = lax.slice_in_dim(shard, 0, width, axis=dim)
        before = lax.ppermute(last, axis, up)
        after = lax.ppermute(initial, axis, down)
        shard = jnp.concatenate([before, shard, after], axis=dim)
    return shard


def neighbours(padded):
    middle = padded[..., 1:-1, 1:-1, :]
    zeros = jnp.zeros(middle.shape[:-1] + (1,), middle.dtype)
    return (
        padded[..., 2:, 1:-1, :],
        padded[..., :-2, 1:-1, :],
        padded[..., 1:-1, 2:, :],
        padded[..., 1:-1, :-2, :],
        jnp.concatenate([middle[..., 1:], zeros], axis=-1),
        jnp.concatenate([zeros, middle[..., :-1]], axis=-1),
    )


def apply(padded, faces, diagonal):
    field = padded[..., 1:-1, 1:-1, :]
    total = diagonal * field
    for weight, near in zip(faces, neighbours(padded)):
        total = total - weight * near
    return total


def gram(left, right):
    return jnp.einsum("axyz,bxyz->ab", left, right, precision=highest)


def combine(coef, field):
    return jnp.einsum("ab,axyz->bxyz", coef, field, precision=highest)


def solve_small(matrix, rhs):
    factor = jnp.linalg.cholesky(matrix)
    middle = lax.linalg.triangular_solve(factor, rhs, left_side=True, lower=True)
    return lax.linalg.triangular_solve(factor, middle, left_side=True, lower=True, transpose_a=True)


def extend(field):
    return with_halo(field, (("gx", 1), ("yz", 2)), 1)


def shifted_sum(value, axis, stride, count):
    size = lax.axis_size(axis)
    total = value
    for step in range(1, count):
        pairs = [(i, (i + stride * step) % size) for i in range(size)]
        total = total + lax.ppermute(value, axis, pairs)
    return total


def reduce_grid(value):
    for axis in ("gx", "yz"):
        size = lax.axis_size(axis)
        stride = 1
        while stride < size:
            value = value + lax.ppermute(value, axis, [(i, i ^ stride) for i in range(size)])
            stride *= 2
    return value


def global_gram(left, right):
    return reduce_grid(gram(left, right))


def scatter_sources(partial_value):
    size = lax.axis_size("src")
    width = partial_value.shape[2] // size
    index = lax.axis_index("src")

    def chunk(offset):
        return lax.dynamic_slice_in_dim(partial_value, ((index + offset) % size) * width, width, axis=2)

    total = chunk(0)
    for step in range(1, size):
        pairs = [(i, (i + step) % size) for i in range(size)]
        total = total + lax.ppermute(chunk(step), "src", pairs)
    return total


def local_sources(count, cells, currents, electrodes, receivers, weights):
    size_x, size_y, size_z = cells
    span_y = size_y * lax.axis_size("yz")
    anchor_x = lax.axis_index("gx") * size_x
    anchor_y = lax.axis_index("yz") * size_y

    def place(index):
        plane = span_y * size_z
        glob_x = index // plane
        glob_y = index % plane // size_z
        glob_z = index % size_z
        loc_x = glob_x - anchor_x
        loc_y = glob_y - anchor_y
        inside = (loc_x >= 0) & (loc_x < size_x) & (loc_y >= 0) & (loc_y < size_y)
        return jnp.where(
            inside, (loc_x * size_y + loc_y) * size_z + glob_z, size_x * size_y * size_z
        )

    local = jnp.arange(count, dtype=jnp.int32)
    field = jnp.zeros((2, count, size_x * size_y * size_z), jnp.float32)
    field = field.at[0, local, place(electrodes[:, 0])].add(currents, mode="drop")
    field = field.at[0, local, place(electrodes[:, 1])].add(-currents, mode="drop")
    field = field.at[1, local[:, None], place(receivers)[None, :]].add(weights, mode="drop")
    return field.reshape((2 * count,) + cells)


def on_device(warm_start, conductivity, currents, electrodes, receivers, weights):
    count = warm_start.shape[1]
    cells = warm_start.shape[2:]
    padded_cond = with_halo(conductivity, (("gx", 0), ("yz", 1)), 1)
    faces = tuple((0.5 * (conductivity + near) for near in neighbours(padded_cond)))
    diagonal = faces[0]
    for weight in faces[1:]:
        diagonal = diagonal + weight
    rhs = local_sources(count, cells, currents, electrodes, receivers, weights)
    solution = warm_start.reshape((2 * count,) + cells)
    padded_solution = extend(solution)
    residual = rhs - apply(padded_solution, faces, diagonal)
    precond = residual / diagonal
    direction = precond
    inner = gram(residual, precond)
    padded_direction = extend(direction)
    image = apply(padded_direction, faces, diagonal)
    inner, curve = reduce_grid(jnp.stack([inner, gram(direction, image)]))
    for step in range(ITERS):
        alpha = solve_small(curve, inner)
        solution = solution + combine(alpha, direction)
        if step + 1 < ITERS:
            residual = residual - combine(alpha, image)
            precond = residual / diagonal
            precond_image = apply(extend(precond), faces, diagonal)
            fresh, self_curve, cross = reduce_grid(jnp.stack(
                [gram(residual, precond), gram(precond, precond_image), gram(precond, image)]))
            beta = solve_small(inner, fresh)
            mixed = jnp.matmul(cross, beta, precision=highest)
            curve = (self_curve + mixed + mixed.T
                     + jnp.matmul(beta.T, jnp.matmul(curve, beta, precision=highest), precision=highest))
            direction = precond + combine(beta, direction)
            image = precond_image + combine(beta, image)
            inner = fresh
    padded_solution = with_halo(solution, (("gx", 1), ("yz", 2)), 1)
    forward = solution[:count]
    adjoint = solution[count:]
    total = jnp.zeros(cells, jnp.float32)
    for near_fwd, near_adj in zip(
        neighbours(padded_solution[:count]), neighbours(padded_solution[count:])
    ):
        total = total + jnp.sum((forward - near_fwd) * (adjoint - near_adj), axis=0)
    partial_value = -0.5 * total
    gradient = scatter_sources(partial_value)
    return (solution.reshape(warm_start.shape), gradient)


def solution(mesh):
    return jax.shard_map(
        on_device,
        mesh=mesh,
        in_specs=(
            P(None, "src", "gx", "yz", None),
            P("gx", "yz", None),
            P("src"),
            P("src", None),
            P(),
            P("src", None),
        ),
        out_specs=(P(None, "src", "gx", "yz", None), P("gx", "yz", "src")),
        check_vma=False,
    )
```

```python
import jax
import jax.numpy as jnp
from jax import lax
from jax.sharding import PartitionSpec as P

ITERS = 2


highest = lax.Precision.HIGHEST


def with_halo(shards, sides, width):
    for axis, dim in sides:
        count, length = (lax.axis_size(axis), shards[0].shape[dim])
        up = [(i, (i + 1) % count) for i in range(count - 1)]
        down = [(j, i) for i, j in up]
        last = jnp.concatenate([lax.slice_in_dim(s, length - width, length, axis=dim) for s in shards])
        initial = jnp.concatenate([lax.slice_in_dim(s, 0, width, axis=dim) for s in shards])
        before = lax.ppermute(last, axis, up)
        after = lax.ppermute(initial, axis, down)
        out = []
        offset = 0
        for s in shards:
            n = s.shape[0]
            out.append(jnp.concatenate([before[offset:offset + n], s, after[offset:offset + n]], axis=dim))
            offset += n
        shards = out
    return shards


def neighbours(padded):
    middle = padded[..., 1:-1, 1:-1, :]
    zeros = jnp.zeros(middle.shape[:-1] + (1,), middle.dtype)
    return (
        padded[..., 2:, 1:-1, :],
        padded[..., :-2, 1:-1, :],
        padded[..., 1:-1, 2:, :],
        padded[..., 1:-1, :-2, :],
        jnp.concatenate([middle[..., 1:], zeros], axis=-1),
        jnp.concatenate([zeros, middle[..., :-1]], axis=-1),
    )


def apply(padded, faces, diagonal):
    field = padded[..., 1:-1, 1:-1, :]
    total = diagonal * field
    for weight, near in zip(faces, neighbours(padded)):
        total = total - weight * near
    return total


def gram(left, right):
    return jnp.einsum("axyz,bxyz->ab", left, right, precision=highest)


def combine(coef, field):
    return jnp.einsum("ab,axyz->bxyz", coef, field, precision=highest)


def solve_small(matrix, rhs):
    factor = jnp.linalg.cholesky(matrix)
    middle = lax.linalg.triangular_solve(factor, rhs, left_side=True, lower=True)
    return lax.linalg.triangular_solve(factor, middle, left_side=True, lower=True, transpose_a=True)


def extend(field):
    return with_halo([field], (("gx", 1), ("yz", 2)), 1)[0]


def shifted_sum(value, axis, stride, count):
    size = lax.axis_size(axis)
    total = value
    for step in range(1, count):
        pairs = [(i, (i + stride * step) % size) for i in range(size)]
        total = total + lax.ppermute(value, axis, pairs)
    return total


def reduce_grid(value):
    value = shifted_sum(value, "gx", 1, lax.axis_size("gx"))
    size = lax.axis_size("yz")
    value = value + lax.ppermute(value, "yz", [(i, i ^ 1) for i in range(size)])
    return shifted_sum(value, "yz", 2, size // 2)


def global_gram(left, right):
    return reduce_grid(gram(left, right))


def scatter_sources(partial_value):
    size = lax.axis_size("src")
    width = partial_value.shape[2] // size
    index = lax.axis_index("src")

    def chunk(offset):
        return lax.dynamic_slice_in_dim(partial_value, ((index + offset) % size) * width, width, axis=2)

    total = chunk(0)
    for step in range(1, size):
        pairs = [(i, (i + step) % size) for i in range(size)]
        total = total + lax.ppermute(chunk(step), "src", pairs)
    return total


def local_sources(count, cells, currents, electrodes, receivers, weights):
    size_x, size_y, size_z = cells
    span_y = size_y * lax.axis_size("yz")
    anchor_x = lax.axis_index("gx") * size_x
    anchor_y = lax.axis_index("yz") * size_y

    def place(index):
        plane = span_y * size_z
        glob_x = index // plane
        glob_y = index % plane // size_z
        glob_z = index % size_z
        loc_x = glob_x - anchor_x
        loc_y = glob_y - anchor_y
        inside = (loc_x >= 0) & (loc_x < size_x) & (loc_y >= 0) & (loc_y < size_y)
        return jnp.where(
            inside, (loc_x * size_y + loc_y) * size_z + glob_z, size_x * size_y * size_z
        )

    local = jnp.arange(count, dtype=jnp.int32)
    field = jnp.zeros((2, count, size_x * size_y * size_z), jnp.float32)
    field = field.at[0, local, place(electrodes[:, 0])].add(currents, mode="drop")
    field = field.at[0, local, place(electrodes[:, 1])].add(-currents, mode="drop")
    field = field.at[1, local[:, None], place(receivers)[None, :]].add(weights, mode="drop")
    return field.reshape((2 * count,) + cells)


def on_device(warm_start, conductivity, currents, electrodes, receivers, weights):
    count = warm_start.shape[1]
    cells = warm_start.shape[2:]
    solution = warm_start.reshape((2 * count,) + cells)
    padded_cond, padded_solution = with_halo([conductivity[None], solution], (("gx", 1), ("yz", 2)), 1)
    padded_cond = padded_cond[0]
    faces = tuple((0.5 * (conductivity + near) for near in neighbours(padded_cond)))
    diagonal = faces[0]
    for weight in faces[1:]:
        diagonal = diagonal + weight
    rhs = local_sources(count, cells, currents, electrodes, receivers, weights)
    residual = rhs - apply(padded_solution, faces, diagonal)
    precond = residual / diagonal
    direction = precond
    inner = gram(residual, precond)
    padded_direction = extend(direction)
    image = apply(padded_direction, faces, diagonal)
    inner, curve = reduce_grid(jnp.stack([inner, gram(direction, image)]))
    for step in range(ITERS):
        alpha = solve_small(curve, inner)
        solution = solution + combine(alpha, direction)
        if step + 1 < ITERS:
            residual = residual - combine(alpha, image)
            precond = residual / diagonal
            precond_image = apply(extend(precond), faces, diagonal)
            fresh, self_curve, cross = reduce_grid(jnp.stack(
                [gram(residual, precond), gram(precond, precond_image), gram(precond, image)]))
            beta = solve_small(inner, fresh)
            mixed = jnp.matmul(cross, beta, precision=highest)
            curve = (self_curve + mixed + mixed.T
                     + jnp.matmul(beta.T, jnp.matmul(curve, beta, precision=highest), precision=highest))
            direction = precond + combine(beta, direction)
            image = precond_image + combine(beta, image)
            inner = fresh
    padded_solution = extend(solution)
    forward = solution[:count]
    adjoint = solution[count:]
    total = jnp.zeros(cells, jnp.float32)
    for near_fwd, near_adj in zip(
        neighbours(padded_solution[:count]), neighbours(padded_solution[count:])
    ):
        total = total + jnp.sum((forward - near_fwd) * (adjoint - near_adj), axis=0)
    partial_value = -0.5 * total
    gradient = scatter_sources(partial_value)
    return (solution.reshape(warm_start.shape), gradient)


def solution(mesh):
    return jax.shard_map(
        on_device,
        mesh=mesh,
        in_specs=(
            P(None, "src", "gx", "yz", None),
            P("gx", "yz", None),
            P("src"),
            P("src", None),
            P(),
            P("src", None),
        ),
        out_specs=(P(None, "src", "gx", "yz", None), P("gx", "yz", "src")),
        check_vma=False,
    )
```

```python
import jax
import jax.numpy as jnp
from jax import lax
from jax.sharding import PartitionSpec as P

ITERS = 2


highest = lax.Precision.HIGHEST


def with_halo(shards, sides, width):
    for axis, dim in sides:
        count, length = (lax.axis_size(axis), shards[0].shape[dim])
        up = [(i, (i + 1) % count) for i in range(count - 1)]
        down = [(j, i) for i, j in up]
        last = jnp.concatenate([lax.slice_in_dim(s, length - width, length, axis=dim) for s in shards])
        initial = jnp.concatenate([lax.slice_in_dim(s, 0, width, axis=dim) for s in shards])
        before = lax.ppermute(last, axis, up)
        after = lax.ppermute(initial, axis, down)
        out = []
        offset = 0
        for s in shards:
            n = s.shape[0]
            out.append(jnp.concatenate([before[offset:offset + n], s, after[offset:offset + n]], axis=dim))
            offset += n
        shards = out
    return shards


def neighbours(padded):
    middle = padded[..., 1:-1, 1:-1, :]
    zeros = jnp.zeros(middle.shape[:-1] + (1,), middle.dtype)
    return (
        padded[..., 2:, 1:-1, :],
        padded[..., :-2, 1:-1, :],
        padded[..., 1:-1, 2:, :],
        padded[..., 1:-1, :-2, :],
        jnp.concatenate([middle[..., 1:], zeros], axis=-1),
        jnp.concatenate([zeros, middle[..., :-1]], axis=-1),
    )


def apply(padded, faces, diagonal):
    field = padded[..., 1:-1, 1:-1, :]
    total = diagonal * field
    for weight, near in zip(faces, neighbours(padded)):
        total = total - weight * near
    return total


def gram(left, right):
    return jnp.einsum("axyz,bxyz->ab", left, right, precision=highest)


def combine(coef, field):
    return jnp.einsum("ab,axyz->bxyz", coef, field, precision=highest)


def solve_small(matrix, rhs):
    factor = jnp.linalg.cholesky(matrix)
    middle = lax.linalg.triangular_solve(factor, rhs, left_side=True, lower=True)
    return lax.linalg.triangular_solve(factor, middle, left_side=True, lower=True, transpose_a=True)


def extend(field):
    return with_halo([field], (("gx", 1), ("yz", 2)), 1)[0]


def combine_plane(coef, plane):
    return jnp.sum(coef[:, :, None, None, None] * plane[:, None], axis=0)


def planes_of(padded):
    return (padded[:, :1], padded[:, -1:], padded[:, :, :1], padded[:, :, -1:])


def add_planes(planes, coef, other):
    return tuple(p + combine_plane(coef, q) for p, q in zip(planes, other))


def padded_from(field, planes):
    x_before, x_after, y_before, y_after = planes
    wide = jnp.concatenate([x_before[:, :, 1:-1], field, x_after[:, :, 1:-1]], axis=1)
    return jnp.concatenate([y_before, wide, y_after], axis=2)


def shifted_sum(value, axis, stride, count):
    size = lax.axis_size(axis)
    total = value
    for step in range(1, count):
        pairs = [(i, (i + stride * step) % size) for i in range(size)]
        total = total + lax.ppermute(value, axis, pairs)
    return total


def reduce_grid(value):
    value = shifted_sum(value, "gx", 1, lax.axis_size("gx"))
    size = lax.axis_size("yz")
    value = value + lax.ppermute(value, "yz", [(i, i ^ 1) for i in range(size)])
    return shifted_sum(value, "yz", 2, size // 2)


def global_gram(left, right):
    return reduce_grid(gram(left, right))


def scatter_sources(partial_value):
    size = lax.axis_size("src")
    width = partial_value.shape[2] // size
    index = lax.axis_index("src")

    def chunk(offset):
        return lax.dynamic_slice_in_dim(partial_value, ((index + offset) % size) * width, width, axis=2)

    total = chunk(0)
    for step in range(1, size):
        pairs = [(i, (i + step) % size) for i in range(size)]
        total = total + lax.ppermute(chunk(step), "src", pairs)
    return total


def local_sources(count, cells, currents, electrodes, receivers, weights):
    size_x, size_y, size_z = cells
    span_y = size_y * lax.axis_size("yz")
    anchor_x = lax.axis_index("gx") * size_x
    anchor_y = lax.axis_index("yz") * size_y

    def place(index):
        plane = span_y * size_z
        glob_x = index // plane
        glob_y = index % plane // size_z
        glob_z = index % size_z
        loc_x = glob_x - anchor_x
        loc_y = glob_y - anchor_y
        inside = (loc_x >= 0) & (loc_x < size_x) & (loc_y >= 0) & (loc_y < size_y)
        return jnp.where(
            inside, (loc_x * size_y + loc_y) * size_z + glob_z, size_x * size_y * size_z
        )

    local = jnp.arange(count, dtype=jnp.int32)
    field = jnp.zeros((2, count, size_x * size_y * size_z), jnp.float32)
    field = field.at[0, local, place(electrodes[:, 0])].add(currents, mode="drop")
    field = field.at[0, local, place(electrodes[:, 1])].add(-currents, mode="drop")
    field = field.at[1, local[:, None], place(receivers)[None, :]].add(weights, mode="drop")
    return field.reshape((2 * count,) + cells)


def on_device(warm_start, conductivity, currents, electrodes, receivers, weights):
    count = warm_start.shape[1]
    cells = warm_start.shape[2:]
    solution = warm_start.reshape((2 * count,) + cells)
    padded_cond, padded_solution = with_halo([conductivity[None], solution], (("gx", 1), ("yz", 2)), 1)
    padded_cond = padded_cond[0]
    faces = tuple((0.5 * (conductivity + near) for near in neighbours(padded_cond)))
    diagonal = faces[0]
    for weight in faces[1:]:
        diagonal = diagonal + weight
    rhs = local_sources(count, cells, currents, electrodes, receivers, weights)
    residual = rhs - apply(padded_solution, faces, diagonal)
    precond = residual / diagonal
    direction = precond
    inner = gram(residual, precond)
    padded_direction = extend(direction)
    image = apply(padded_direction, faces, diagonal)
    inner, curve = reduce_grid(jnp.stack([inner, gram(direction, image)]))
    solution_planes = planes_of(padded_solution)
    direction_planes = planes_of(padded_direction)
    for step in range(ITERS):
        alpha = solve_small(curve, inner)
        solution = solution + combine(alpha, direction)
        solution_planes = add_planes(solution_planes, alpha, direction_planes)
        if step + 1 < ITERS:
            residual = residual - combine(alpha, image)
            precond = residual / diagonal
            padded_precond = extend(precond)
            precond_image = apply(padded_precond, faces, diagonal)
            fresh, self_curve, cross = reduce_grid(jnp.stack(
                [gram(residual, precond), gram(precond, precond_image), gram(precond, image)]))
            beta = solve_small(inner, fresh)
            mixed = jnp.matmul(cross, beta, precision=highest)
            curve = (self_curve + mixed + mixed.T
                     + jnp.matmul(beta.T, jnp.matmul(curve, beta, precision=highest), precision=highest))
            direction = precond + combine(beta, direction)
            direction_planes = add_planes(planes_of(padded_precond), beta, direction_planes)
            image = precond_image + combine(beta, image)
            inner = fresh
    padded_solution = padded_from(solution, solution_planes)
    forward = solution[:count]
    adjoint = solution[count:]
    total = jnp.zeros(cells, jnp.float32)
    for near_fwd, near_adj in zip(
        neighbours(padded_solution[:count]), neighbours(padded_solution[count:])
    ):
        total = total + jnp.sum((forward - near_fwd) * (adjoint - near_adj), axis=0)
    partial_value = -0.5 * total
    gradient = scatter_sources(partial_value)
    return (solution.reshape(warm_start.shape), gradient)


def solution(mesh):
    return jax.shard_map(
        on_device,
        mesh=mesh,
        in_specs=(
            P(None, "src", "gx", "yz", None),
            P("gx", "yz", None),
            P("src"),
            P("src", None),
            P(),
            P("src", None),
        ),
        out_specs=(P(None, "src", "gx", "yz", None), P("gx", "yz", "src")),
        check_vma=False,
    )
```

```python
import jax
import jax.numpy as jnp
from jax import lax
from jax.sharding import PartitionSpec as P

ITERS = 2


highest = lax.Precision.HIGHEST


def with_halo(shards, sides, width):
    received = []
    for axis, dim in sides:
        count, length = (lax.axis_size(axis), shards[0].shape[dim])
        up = [(i, (i + 1) % count) for i in range(count - 1)]
        down = [(j, i) for i, j in up]
        last = jnp.concatenate([lax.slice_in_dim(s, length - width, length, axis=dim) for s in shards])
        initial = jnp.concatenate([lax.slice_in_dim(s, 0, width, axis=dim) for s in shards])
        received.append((dim, lax.ppermute(last, axis, up), lax.ppermute(initial, axis, down)))
    done = []
    for (dim, before, after) in received:
        widths = [(0, 0)] * before.ndim
        for other, _, _ in done:
            widths[other] = (width, width)
        before, after = jnp.pad(before, widths), jnp.pad(after, widths)
        out = []
        offset = 0
        for s in shards:
            n = s.shape[0]
            out.append(jnp.concatenate([before[offset:offset + n], s, after[offset:offset + n]], axis=dim))
            offset += n
        shards = out
        done.append((dim, before, after))
    return shards


def neighbours(padded):
    middle = padded[..., 1:-1, 1:-1, :]
    zeros = jnp.zeros(middle.shape[:-1] + (1,), middle.dtype)
    return (
        padded[..., 2:, 1:-1, :],
        padded[..., :-2, 1:-1, :],
        padded[..., 1:-1, 2:, :],
        padded[..., 1:-1, :-2, :],
        jnp.concatenate([middle[..., 1:], zeros], axis=-1),
        jnp.concatenate([zeros, middle[..., :-1]], axis=-1),
    )


def apply(padded, faces, diagonal):
    field = padded[..., 1:-1, 1:-1, :]
    total = diagonal * field
    for weight, near in zip(faces, neighbours(padded)):
        total = total - weight * near
    return total


def gram(left, right):
    return jnp.einsum("axyz,bxyz->ab", left, right, precision=highest)


def combine(coef, field):
    return jnp.einsum("ab,axyz->bxyz", coef, field, precision=highest)


def solve_small(matrix, rhs):
    factor = jnp.linalg.cholesky(matrix)
    middle = lax.linalg.triangular_solve(factor, rhs, left_side=True, lower=True)
    return lax.linalg.triangular_solve(factor, middle, left_side=True, lower=True, transpose_a=True)


def extend(field):
    return with_halo([field], (("gx", 1), ("yz", 2)), 1)[0]


def combine_plane(coef, plane):
    return jnp.sum(coef[:, :, None, None, None] * plane[:, None], axis=0)


def planes_of(padded):
    return (padded[:, :1], padded[:, -1:], padded[:, :, :1], padded[:, :, -1:])


def add_planes(planes, coef, other):
    return tuple(p + combine_plane(coef, q) for p, q in zip(planes, other))


def padded_from(field, planes):
    x_before, x_after, y_before, y_after = planes
    wide = jnp.concatenate([x_before[:, :, 1:-1], field, x_after[:, :, 1:-1]], axis=1)
    return jnp.concatenate([y_before, wide, y_after], axis=2)


def shifted_sum(value, axis, stride, count):
    size = lax.axis_size(axis)
    total = value
    for step in range(1, count):
        pairs = [(i, (i + stride * step) % size) for i in range(size)]
        total = total + lax.ppermute(value, axis, pairs)
    return total


def reduce_grid(value):
    value = shifted_sum(value, "gx", 1, lax.axis_size("gx"))
    size = lax.axis_size("yz")
    value = value + lax.ppermute(value, "yz", [(i, i ^ 1) for i in range(size)])
    return shifted_sum(value, "yz", 2, size // 2)


def global_gram(left, right):
    return reduce_grid(gram(left, right))


def scatter_sources(partial_value):
    size = lax.axis_size("src")
    width = partial_value.shape[2] // size
    index = lax.axis_index("src")

    def chunk(offset):
        return lax.dynamic_slice_in_dim(partial_value, ((index + offset) % size) * width, width, axis=2)

    total = chunk(0)
    for step in range(1, size):
        pairs = [(i, (i + step) % size) for i in range(size)]
        total = total + lax.ppermute(chunk(step), "src", pairs)
    return total


def local_sources(count, cells, currents, electrodes, receivers, weights):
    size_x, size_y, size_z = cells
    span_y = size_y * lax.axis_size("yz")
    anchor_x = lax.axis_index("gx") * size_x
    anchor_y = lax.axis_index("yz") * size_y

    def place(index):
        plane = span_y * size_z
        glob_x = index // plane
        glob_y = index % plane // size_z
        glob_z = index % size_z
        loc_x = glob_x - anchor_x
        loc_y = glob_y - anchor_y
        inside = (loc_x >= 0) & (loc_x < size_x) & (loc_y >= 0) & (loc_y < size_y)
        return jnp.where(
            inside, (loc_x * size_y + loc_y) * size_z + glob_z, size_x * size_y * size_z
        )

    local = jnp.arange(count, dtype=jnp.int32)
    field = jnp.zeros((2, count, size_x * size_y * size_z), jnp.float32)
    field = field.at[0, local, place(electrodes[:, 0])].add(currents, mode="drop")
    field = field.at[0, local, place(electrodes[:, 1])].add(-currents, mode="drop")
    field = field.at[1, local[:, None], place(receivers)[None, :]].add(weights, mode="drop")
    return field.reshape((2 * count,) + cells)


def on_device(warm_start, conductivity, currents, electrodes, receivers, weights):
    count = warm_start.shape[1]
    cells = warm_start.shape[2:]
    solution = warm_start.reshape((2 * count,) + cells)
    padded_cond, padded_solution = with_halo([conductivity[None], solution], (("gx", 1), ("yz", 2)), 1)
    padded_cond = padded_cond[0]
    faces = tuple((0.5 * (conductivity + near) for near in neighbours(padded_cond)))
    diagonal = faces[0]
    for weight in faces[1:]:
        diagonal = diagonal + weight
    rhs = local_sources(count, cells, currents, electrodes, receivers, weights)
    residual = rhs - apply(padded_solution, faces, diagonal)
    precond = residual / diagonal
    direction = precond
    inner = gram(residual, precond)
    padded_direction = extend(direction)
    image = apply(padded_direction, faces, diagonal)
    inner, curve = reduce_grid(jnp.stack([inner, gram(direction, image)]))
    solution_planes = planes_of(padded_solution)
    direction_planes = planes_of(padded_direction)
    for step in range(ITERS):
        alpha = solve_small(curve, inner)
        solution = solution + combine(alpha, direction)
        solution_planes = add_planes(solution_planes, alpha, direction_planes)
        if step + 1 < ITERS:
            residual = residual - combine(alpha, image)
            precond = residual / diagonal
            padded_precond = extend(precond)
            precond_image = apply(padded_precond, faces, diagonal)
            fresh, self_curve, cross = reduce_grid(jnp.stack(
                [gram(residual, precond), gram(precond, precond_image), gram(precond, image)]))
            beta = solve_small(inner, fresh)
            mixed = jnp.matmul(cross, beta, precision=highest)
            curve = (self_curve + mixed + mixed.T
                     + jnp.matmul(beta.T, jnp.matmul(curve, beta, precision=highest), precision=highest))
            direction = precond + combine(beta, direction)
            direction_planes = add_planes(planes_of(padded_precond), beta, direction_planes)
            image = precond_image + combine(beta, image)
            inner = fresh
    padded_solution = padded_from(solution, solution_planes)
    forward = solution[:count]
    adjoint = solution[count:]
    total = jnp.zeros(cells, jnp.float32)
    for near_fwd, near_adj in zip(
        neighbours(padded_solution[:count]), neighbours(padded_solution[count:])
    ):
        total = total + jnp.sum((forward - near_fwd) * (adjoint - near_adj), axis=0)
    partial_value = -0.5 * total
    gradient = scatter_sources(partial_value)
    return (solution.reshape(warm_start.shape), gradient)


def solution(mesh):
    return jax.shard_map(
        on_device,
        mesh=mesh,
        in_specs=(
            P(None, "src", "gx", "yz", None),
            P("gx", "yz", None),
            P("src"),
            P("src", None),
            P(),
            P("src", None),
        ),
        out_specs=(P(None, "src", "gx", "yz", None), P("gx", "yz", "src")),
        check_vma=False,
    )
```

```python
import jax
import jax.numpy as jnp
from jax import lax
from jax.sharding import PartitionSpec as P

ITERS = 2


highest = lax.Precision.HIGHEST


def with_halo(shards, sides, width):
    received = []
    for axis, dim in sides:
        count, length = (lax.axis_size(axis), shards[0].shape[dim])
        up = [(i, (i + 1) % count) for i in range(count - 1)]
        down = [(j, i) for i, j in up]
        last = jnp.concatenate([lax.slice_in_dim(s, length - width, length, axis=dim) for s in shards])
        initial = jnp.concatenate([lax.slice_in_dim(s, 0, width, axis=dim) for s in shards])
        received.append((dim, lax.ppermute(last, axis, up), lax.ppermute(initial, axis, down)))
    done = []
    for (dim, before, after) in received:
        widths = [(0, 0)] * before.ndim
        for other, _, _ in done:
            widths[other] = (width, width)
        before, after = jnp.pad(before, widths), jnp.pad(after, widths)
        out = []
        offset = 0
        for s in shards:
            n = s.shape[0]
            out.append(jnp.concatenate([before[offset:offset + n], s, after[offset:offset + n]], axis=dim))
            offset += n
        shards = out
        done.append((dim, before, after))
    return shards


def neighbours(padded):
    middle = padded[..., 1:-1, 1:-1, :]
    zeros = jnp.zeros(middle.shape[:-1] + (1,), middle.dtype)
    return (
        padded[..., 2:, 1:-1, :],
        padded[..., :-2, 1:-1, :],
        padded[..., 1:-1, 2:, :],
        padded[..., 1:-1, :-2, :],
        jnp.concatenate([middle[..., 1:], zeros], axis=-1),
        jnp.concatenate([zeros, middle[..., :-1]], axis=-1),
    )


def apply(padded, faces, diagonal):
    field = padded[..., 1:-1, 1:-1, :]
    total = diagonal * field
    for weight, near in zip(faces, neighbours(padded)):
        total = total - weight * near
    return total


def gram(left, right):
    return jnp.einsum("axyz,bxyz->ab", left, right, precision=highest)


def combine(coef, field):
    return jnp.einsum("ab,axyz->bxyz", coef, field, precision=highest)


def solve_small(matrix, rhs):
    factor = jnp.linalg.cholesky(matrix)
    middle = lax.linalg.triangular_solve(factor, rhs, left_side=True, lower=True)
    return lax.linalg.triangular_solve(factor, middle, left_side=True, lower=True, transpose_a=True)


def extend(field):
    return with_halo([field], (("gx", 1), ("yz", 2)), 1)[0]


def combine_plane(coef, plane):
    return jnp.sum(coef[:, :, None, None, None] * plane[:, None], axis=0)


def planes_of(padded):
    return (padded[:, :1], padded[:, -1:], padded[:, :, :1], padded[:, :, -1:])


def add_planes(planes, coef, other):
    return tuple(p + combine_plane(coef, q) for p, q in zip(planes, other))


def padded_from(field, planes):
    x_before, x_after, y_before, y_after = planes
    wide = jnp.concatenate([x_before[:, :, 1:-1], field, x_after[:, :, 1:-1]], axis=1)
    return jnp.concatenate([y_before, wide, y_after], axis=2)


def shifted_sum(value, axis, stride, count):
    size = lax.axis_size(axis)
    total = value
    for step in range(1, count):
        pairs = [(i, (i + stride * step) % size) for i in range(size)]
        total = total + lax.ppermute(value, axis, pairs)
    return total


def reduce_grid(value):
    value = shifted_sum(value, "gx", 1, lax.axis_size("gx"))
    size = lax.axis_size("yz")
    value = value + lax.ppermute(value, "yz", [(i, i ^ 1) for i in range(size)])
    return shifted_sum(value, "yz", 2, size // 2)


def global_gram(left, right):
    return reduce_grid(gram(left, right))


def scatter_sources(partial_value):
    size = lax.axis_size("src")
    width = partial_value.shape[2] // size
    index = lax.axis_index("src")

    def chunk(offset):
        return lax.dynamic_slice_in_dim(partial_value, ((index + offset) % size) * width, width, axis=2)

    total = chunk(0)
    for step in range(1, size):
        pairs = [(i, (i + step) % size) for i in range(size)]
        total = total + lax.ppermute(chunk(step), "src", pairs)
    return total


def local_sources(count, cells, currents, electrodes, receivers, weights):
    size_x, size_y, size_z = cells
    lanes = 128 if size_z % 128 == 0 else size_z
    span_y = size_y * lax.axis_size("yz")
    anchor_x = lax.axis_index("gx") * size_x
    anchor_y = lax.axis_index("yz") * size_y
    columns = 2 * count
    total = columns * size_x * size_y * size_z

    def place(index, column):
        plane = span_y * size_z
        loc_x = index // plane - anchor_x
        loc_y = index % plane // size_z - anchor_y
        loc_z = index % size_z
        inside = (loc_x >= 0) & (loc_x < size_x) & (loc_y >= 0) & (loc_y < size_y)
        spot = (((loc_x * size_y + loc_y) * (size_z // lanes) + loc_z // lanes) * columns + column) * lanes + loc_z % lanes
        return jnp.where(inside, spot, total)

    local = jnp.arange(count, dtype=jnp.int32)
    field = jnp.zeros((total,), jnp.float32)
    field = field.at[place(electrodes[:, 0], local)].add(currents, mode="drop")
    field = field.at[place(electrodes[:, 1], local)].add(-currents, mode="drop")
    field = field.at[place(receivers[None, :], count + local[:, None])].add(weights, mode="drop")
    field = field.reshape(size_x, size_y, size_z // lanes, columns, lanes)
    return jnp.transpose(field, (3, 0, 1, 2, 4)).reshape((columns,) + cells)


def on_device(warm_start, conductivity, currents, electrodes, receivers, weights):
    count = warm_start.shape[1]
    cells = warm_start.shape[2:]
    solution = warm_start.reshape((2 * count,) + cells)
    padded_cond, padded_solution = with_halo([conductivity[None], solution], (("gx", 1), ("yz", 2)), 1)
    padded_cond = padded_cond[0]
    faces = tuple((0.5 * (conductivity + near) for near in neighbours(padded_cond)))
    diagonal = faces[0]
    for weight in faces[1:]:
        diagonal = diagonal + weight
    rhs = local_sources(count, cells, currents, electrodes, receivers, weights)
    residual = rhs - apply(padded_solution, faces, diagonal)
    precond = residual / diagonal
    direction = precond
    inner = gram(residual, precond)
    padded_direction = extend(direction)
    image = apply(padded_direction, faces, diagonal)
    inner, curve = reduce_grid(jnp.stack([inner, gram(direction, image)]))
    solution_planes = planes_of(padded_solution)
    direction_planes = planes_of(padded_direction)
    for step in range(ITERS):
        alpha = solve_small(curve, inner)
        solution = solution + combine(alpha, direction)
        solution_planes = add_planes(solution_planes, alpha, direction_planes)
        if step + 1 < ITERS:
            residual = residual - combine(alpha, image)
            precond = residual / diagonal
            padded_precond = extend(precond)
            precond_image = apply(padded_precond, faces, diagonal)
            fresh, self_curve, cross = reduce_grid(jnp.stack(
                [gram(residual, precond), gram(precond, precond_image), gram(precond, image)]))
            beta = solve_small(inner, fresh)
            mixed = jnp.matmul(cross, beta, precision=highest)
            curve = (self_curve + mixed + mixed.T
                     + jnp.matmul(beta.T, jnp.matmul(curve, beta, precision=highest), precision=highest))
            direction = precond + combine(beta, direction)
            direction_planes = add_planes(planes_of(padded_precond), beta, direction_planes)
            image = precond_image + combine(beta, image)
            inner = fresh
    padded_solution = padded_from(solution, solution_planes)
    forward = solution[:count]
    adjoint = solution[count:]
    total = jnp.zeros(cells, jnp.float32)
    for near_fwd, near_adj in zip(
        neighbours(padded_solution[:count]), neighbours(padded_solution[count:])
    ):
        total = total + jnp.sum((forward - near_fwd) * (adjoint - near_adj), axis=0)
    partial_value = -0.5 * total
    gradient = scatter_sources(partial_value)
    return (solution.reshape(warm_start.shape), gradient)


def solution(mesh):
    return jax.shard_map(
        on_device,
        mesh=mesh,
        in_specs=(
            P(None, "src", "gx", "yz", None),
            P("gx", "yz", None),
            P("src"),
            P("src", None),
            P(),
            P("src", None),
        ),
        out_specs=(P(None, "src", "gx", "yz", None), P("gx", "yz", "src")),
        check_vma=False,
    )
```

```python
import jax
import jax.numpy as jnp
from jax import lax
from jax.sharding import PartitionSpec as P

ITERS = 2


highest = lax.Precision.HIGHEST


def with_halo(shards, sides, width):
    received = []
    for axis, dim in sides:
        count, length = (lax.axis_size(axis), shards[0].shape[dim])
        up = [(i, (i + 1) % count) for i in range(count - 1)]
        down = [(j, i) for i, j in up]
        last = jnp.concatenate([lax.slice_in_dim(s, length - width, length, axis=dim) for s in shards])
        initial = jnp.concatenate([lax.slice_in_dim(s, 0, width, axis=dim) for s in shards])
        received.append((dim, lax.ppermute(last, axis, up), lax.ppermute(initial, axis, down)))
    done = []
    for (dim, before, after) in received:
        widths = [(0, 0)] * before.ndim
        for other, _, _ in done:
            widths[other] = (width, width)
        before, after = jnp.pad(before, widths), jnp.pad(after, widths)
        out = []
        offset = 0
        for s in shards:
            n = s.shape[0]
            out.append(jnp.concatenate([before[offset:offset + n], s, after[offset:offset + n]], axis=dim))
            offset += n
        shards = out
        done.append((dim, before, after))
    return shards


def neighbours(padded):
    middle = padded[..., 1:-1, 1:-1, :]
    zeros = jnp.zeros(middle.shape[:-1] + (1,), middle.dtype)
    return (
        padded[..., 2:, 1:-1, :],
        padded[..., :-2, 1:-1, :],
        padded[..., 1:-1, 2:, :],
        padded[..., 1:-1, :-2, :],
        jnp.concatenate([middle[..., 1:], zeros], axis=-1),
        jnp.concatenate([zeros, middle[..., :-1]], axis=-1),
    )


def apply(padded, faces, diagonal):
    field = padded[..., 1:-1, 1:-1, :]
    total = diagonal * field
    for weight, near in zip(faces, neighbours(padded)):
        total = total - weight * near
    return total


def gram(left, right):
    return jnp.einsum("axyz,bxyz->ab", left, right, precision=highest)


def combine(coef, field):
    return jnp.einsum("ab,axyz->bxyz", coef, field, precision=highest)


def solve_small(matrix, rhs):
    factor = jnp.linalg.cholesky(matrix)
    middle = lax.linalg.triangular_solve(factor, rhs, left_side=True, lower=True)
    return lax.linalg.triangular_solve(factor, middle, left_side=True, lower=True, transpose_a=True)


def extend(field):
    return with_halo([field], (("gx", 1), ("yz", 2)), 1)[0]


def combine_plane(coef, plane):
    return jnp.sum(coef[:, :, None, None, None] * plane[:, None], axis=0)


def planes_of(padded):
    return (padded[:, :1], padded[:, -1:], padded[:, :, :1], padded[:, :, -1:])


def add_planes(planes, coef, other):
    return tuple(p + combine_plane(coef, q) for p, q in zip(planes, other))


def padded_from(field, planes):
    x_before, x_after, y_before, y_after = planes
    wide = jnp.concatenate([x_before[:, :, 1:-1], field, x_after[:, :, 1:-1]], axis=1)
    return jnp.concatenate([y_before, wide, y_after], axis=2)


def shifted_sum(value, axis, stride, count):
    size = lax.axis_size(axis)
    total = value
    for step in range(1, count):
        pairs = [(i, (i + stride * step) % size) for i in range(size)]
        total = total + lax.ppermute(value, axis, pairs)
    return total


def reduce_grid(value):
    value = shifted_sum(value, "gx", 1, lax.axis_size("gx"))
    size = lax.axis_size("yz")
    value = value + lax.ppermute(value, "yz", [(i, i ^ 1) for i in range(size)])
    return shifted_sum(value, "yz", 2, size // 2)


def global_gram(left, right):
    return reduce_grid(gram(left, right))


def scatter_sources(partial_value):
    size = lax.axis_size("src")
    width = partial_value.shape[2] // size
    index = lax.axis_index("src")

    def chunk(offset):
        return lax.dynamic_slice_in_dim(partial_value, ((index + offset) % size) * width, width, axis=2)

    total = chunk(0)
    for step in range(1, size):
        pairs = [(i, (i + step) % size) for i in range(size)]
        total = total + lax.ppermute(chunk(step), "src", pairs)
    return total


def local_sources(count, cells, currents, electrodes, receivers, weights):
    size_x, size_y, size_z = cells
    lanes = 128 if size_z % 128 == 0 else size_z
    span_y = size_y * lax.axis_size("yz")
    anchor_x = lax.axis_index("gx") * size_x
    anchor_y = lax.axis_index("yz") * size_y
    columns = 2 * count
    total = columns * size_x * size_y * size_z

    def place(index, column):
        plane = span_y * size_z
        loc_x = index // plane - anchor_x
        loc_y = index % plane // size_z - anchor_y
        loc_z = index % size_z
        inside = (loc_x >= 0) & (loc_x < size_x) & (loc_y >= 0) & (loc_y < size_y)
        spot = (((loc_x * size_y + loc_y) * (size_z // lanes) + loc_z // lanes) * columns + column) * lanes + loc_z % lanes
        return jnp.where(inside, spot, total)

    local = jnp.arange(count, dtype=jnp.int32)
    spots = jnp.concatenate([
        place(electrodes[:, 0], local),
        place(electrodes[:, 1], local),
        place(receivers[None, :], count + local[:, None]).reshape(-1),
    ])
    values = jnp.concatenate([currents, -currents, weights.reshape(-1)])
    field = jnp.zeros((total,), jnp.float32).at[spots].add(values, mode="drop")
    field = field.reshape(size_x, size_y, size_z // lanes, columns, lanes)
    return jnp.transpose(field, (3, 0, 1, 2, 4)).reshape((columns,) + cells)


def on_device(warm_start, conductivity, currents, electrodes, receivers, weights):
    count = warm_start.shape[1]
    cells = warm_start.shape[2:]
    solution = warm_start.reshape((2 * count,) + cells)
    padded_cond, padded_solution = with_halo([conductivity[None], solution], (("gx", 1), ("yz", 2)), 1)
    padded_cond = padded_cond[0]
    faces = tuple((0.5 * (conductivity + near) for near in neighbours(padded_cond)))
    diagonal = faces[0]
    for weight in faces[1:]:
        diagonal = diagonal + weight
    rhs = local_sources(count, cells, currents, electrodes, receivers, weights)
    residual = rhs - apply(padded_solution, faces, diagonal)
    precond = residual / diagonal
    direction = precond
    inner = gram(residual, precond)
    padded_direction = extend(direction)
    image = apply(padded_direction, faces, diagonal)
    inner, curve = reduce_grid(jnp.stack([inner, gram(direction, image)]))
    solution_planes = planes_of(padded_solution)
    direction_planes = planes_of(padded_direction)
    for step in range(ITERS):
        alpha = solve_small(curve, inner)
        solution = solution + combine(alpha, direction)
        solution_planes = add_planes(solution_planes, alpha, direction_planes)
        if step + 1 < ITERS:
            residual = residual - combine(alpha, image)
            precond = residual / diagonal
            padded_precond = extend(precond)
            precond_image = apply(padded_precond, faces, diagonal)
            fresh, self_curve, cross = reduce_grid(jnp.stack(
                [gram(residual, precond), gram(precond, precond_image), gram(precond, image)]))
            beta = solve_small(inner, fresh)
            mixed = jnp.matmul(cross, beta, precision=highest)
            curve = (self_curve + mixed + mixed.T
                     + jnp.matmul(beta.T, jnp.matmul(curve, beta, precision=highest), precision=highest))
            direction = precond + combine(beta, direction)
            direction_planes = add_planes(planes_of(padded_precond), beta, direction_planes)
            image = precond_image + combine(beta, image)
            inner = fresh
    padded_solution = padded_from(solution, solution_planes)
    forward = solution[:count]
    adjoint = solution[count:]
    total = jnp.zeros(cells, jnp.float32)
    for near_fwd, near_adj in zip(
        neighbours(padded_solution[:count]), neighbours(padded_solution[count:])
    ):
        total = total + jnp.sum((forward - near_fwd) * (adjoint - near_adj), axis=0)
    partial_value = -0.5 * total
    gradient = scatter_sources(partial_value)
    return (solution.reshape(warm_start.shape), gradient)


def solution(mesh):
    return jax.shard_map(
        on_device,
        mesh=mesh,
        in_specs=(
            P(None, "src", "gx", "yz", None),
            P("gx", "yz", None),
            P("src"),
            P("src", None),
            P(),
            P("src", None),
        ),
        out_specs=(P(None, "src", "gx", "yz", None), P("gx", "yz", "src")),
        check_vma=False,
    )
```

```python
import jax
import jax.numpy as jnp
from jax import lax
from jax.sharding import PartitionSpec as P

ITERS = 2


highest = lax.Precision.HIGHEST


def with_halo(shards, sides, width):
    received = []
    for axis, dim in sides:
        count, length = (lax.axis_size(axis), shards[0].shape[dim])
        up = [(i, (i + 1) % count) for i in range(count - 1)]
        down = [(j, i) for i, j in up]
        last = jnp.concatenate([lax.slice_in_dim(s, length - width, length, axis=dim) for s in shards])
        initial = jnp.concatenate([lax.slice_in_dim(s, 0, width, axis=dim) for s in shards])
        received.append((dim, lax.ppermute(last, axis, up), lax.ppermute(initial, axis, down)))
    done = []
    for (dim, before, after) in received:
        widths = [(0, 0)] * before.ndim
        for other, _, _ in done:
            widths[other] = (width, width)
        before, after = jnp.pad(before, widths), jnp.pad(after, widths)
        out = []
        offset = 0
        for s in shards:
            n = s.shape[0]
            out.append(jnp.concatenate([before[offset:offset + n], s, after[offset:offset + n]], axis=dim))
            offset += n
        shards = out
        done.append((dim, before, after))
    return shards


def neighbours(padded):
    middle = padded[..., 1:-1, 1:-1, :]
    zeros = jnp.zeros(middle.shape[:-1] + (1,), middle.dtype)
    return (
        padded[..., 2:, 1:-1, :],
        padded[..., :-2, 1:-1, :],
        padded[..., 1:-1, 2:, :],
        padded[..., 1:-1, :-2, :],
        jnp.concatenate([middle[..., 1:], zeros], axis=-1),
        jnp.concatenate([zeros, middle[..., :-1]], axis=-1),
    )


def apply(padded, faces, diagonal):
    field = padded[..., 1:-1, 1:-1, :]
    total = diagonal * field
    for weight, near in zip(faces, neighbours(padded)):
        total = total - weight * near
    return total


def gram(left, right):
    return jnp.einsum("axyz,bxyz->ab", left, right, precision=highest)


def combine(coef, field):
    return jnp.einsum("ab,axyz->bxyz", coef, field, precision=highest)


def solve_small(matrix, rhs):
    factor = jnp.linalg.cholesky(matrix)
    middle = lax.linalg.triangular_solve(factor, rhs, left_side=True, lower=True)
    return lax.linalg.triangular_solve(factor, middle, left_side=True, lower=True, transpose_a=True)


def extend(field):
    return with_halo([field], (("gx", 1), ("yz", 2)), 1)[0]


def combine_plane(coef, plane):
    return jnp.sum(coef[:, :, None, None, None] * plane[:, None], axis=0)


def planes_of(padded):
    return (padded[:, :1], padded[:, -1:], padded[:, :, :1], padded[:, :, -1:])


def add_planes(planes, coef, other):
    return tuple(p + combine_plane(coef, q) for p, q in zip(planes, other))


def padded_from(field, planes):
    x_before, x_after, y_before, y_after = planes
    wide = jnp.concatenate([x_before[:, :, 1:-1], field, x_after[:, :, 1:-1]], axis=1)
    return jnp.concatenate([y_before, wide, y_after], axis=2)


def shifted_sum(value, axis, stride, count):
    size = lax.axis_size(axis)
    total = value
    for step in range(1, count):
        pairs = [(i, (i + stride * step) % size) for i in range(size)]
        total = total + lax.ppermute(value, axis, pairs)
    return total


def reduce_grid(value):
    value = shifted_sum(value, "gx", 1, lax.axis_size("gx"))
    size = lax.axis_size("yz")
    value = value + lax.ppermute(value, "yz", [(i, i ^ 1) for i in range(size)])
    return shifted_sum(value, "yz", 2, size // 2)


def global_gram(left, right):
    return reduce_grid(gram(left, right))


def scatter_sources(partial_value):
    size = lax.axis_size("src")
    width = partial_value.shape[2] // size
    index = lax.axis_index("src")

    def chunk(offset):
        return lax.dynamic_slice_in_dim(partial_value, ((index + offset) % size) * width, width, axis=2)

    total = chunk(0)
    for step in range(1, size):
        pairs = [(i, (i + step) % size) for i in range(size)]
        total = total + lax.ppermute(chunk(step), "src", pairs)
    return total


def local_sources(count, cells, currents, electrodes, receivers, weights):
    size_x, size_y, size_z = cells
    lanes = 128 if size_z % 128 == 0 else size_z
    span_y = size_y * lax.axis_size("yz")
    anchor_x = lax.axis_index("gx") * size_x
    anchor_y = lax.axis_index("yz") * size_y
    columns = 2 * count
    total = columns * size_x * size_y * size_z

    def place(index, column):
        plane = span_y * size_z
        loc_x = index // plane - anchor_x
        loc_y = index % plane // size_z - anchor_y
        loc_z = index % size_z
        inside = (loc_x >= 0) & (loc_x < size_x) & (loc_y >= 0) & (loc_y < size_y)
        spot = (((loc_x * size_y + loc_y) * (size_z // lanes) + loc_z // lanes) * columns + column) * lanes + loc_z % lanes
        return jnp.where(inside, spot, total)

    local = jnp.arange(count, dtype=jnp.int32)
    spots = jnp.concatenate([
        place(electrodes[:, 0], local),
        place(electrodes[:, 1], local),
        place(receivers[None, :], count + local[:, None]).reshape(-1),
    ])
    values = jnp.concatenate([currents, -currents, weights.reshape(-1)])
    field = jnp.zeros((total,), jnp.float32).at[spots].add(values, mode="drop")
    field = field.reshape(size_x, size_y, size_z // lanes, columns, lanes)
    return jnp.transpose(field, (3, 0, 1, 2, 4)).reshape((columns,) + cells)


def on_device(warm_start, conductivity, currents, electrodes, receivers, weights):
    count = warm_start.shape[1]
    cells = warm_start.shape[2:]
    solution = warm_start.reshape((2 * count,) + cells)
    padded_cond, padded_solution = with_halo([conductivity[None], solution], (("gx", 1), ("yz", 2)), 1)
    padded_cond = padded_cond[0]
    faces = tuple((0.5 * (conductivity + near) for near in neighbours(padded_cond)))
    diagonal = faces[0]
    for weight in faces[1:]:
        diagonal = diagonal + weight
    rhs = local_sources(count, cells, currents, electrodes, receivers, weights)
    residual = rhs - apply(padded_solution, faces, diagonal)
    precond = residual / diagonal
    direction = precond
    inner = gram(residual, precond)
    padded_direction = extend(direction)
    image = apply(padded_direction, faces, diagonal)
    inner, curve = reduce_grid(jnp.stack([inner, gram(direction, image)]))
    solution_planes = planes_of(padded_solution)
    direction_planes = planes_of(padded_direction)
    alpha = solve_small(curve, inner)
    residual = residual - combine(alpha, image)
    precond = residual / diagonal
    padded_precond = extend(precond)
    precond_image = apply(padded_precond, faces, diagonal)
    fresh, self_curve, cross = reduce_grid(jnp.stack(
        [gram(residual, precond), gram(precond, precond_image), gram(precond, image)]))
    beta = solve_small(inner, fresh)
    mixed = jnp.matmul(cross, beta, precision=highest)
    curve = (self_curve + mixed + mixed.T
             + jnp.matmul(beta.T, jnp.matmul(curve, beta, precision=highest), precision=highest))
    last = solve_small(curve, fresh)
    first = alpha + jnp.matmul(beta, last, precision=highest)
    solution = solution + combine(first, direction) + combine(last, precond)
    solution_planes = add_planes(add_planes(solution_planes, first, direction_planes), last, planes_of(padded_precond))
    padded_solution = padded_from(solution, solution_planes)
    forward = solution[:count]
    adjoint = solution[count:]
    total = jnp.zeros(cells, jnp.float32)
    for near_fwd, near_adj in zip(
        neighbours(padded_solution[:count]), neighbours(padded_solution[count:])
    ):
        total = total + jnp.sum((forward - near_fwd) * (adjoint - near_adj), axis=0)
    partial_value = -0.5 * total
    gradient = scatter_sources(partial_value)
    return (solution.reshape(warm_start.shape), gradient)


def solution(mesh):
    return jax.shard_map(
        on_device,
        mesh=mesh,
        in_specs=(
            P(None, "src", "gx", "yz", None),
            P("gx", "yz", None),
            P("src"),
            P("src", None),
            P(),
            P("src", None),
        ),
        out_specs=(P(None, "src", "gx", "yz", None), P("gx", "yz", "src")),
        check_vma=False,
    )
```

```python
import jax
import jax.numpy as jnp
from jax import lax
from jax.sharding import PartitionSpec as P

ITERS = 2


highest = lax.Precision.HIGHEST


def with_halo(shards, sides, width):
    received = []
    for axis, dim in sides:
        count, length = (lax.axis_size(axis), shards[0].shape[dim])
        up = [(i, (i + 1) % count) for i in range(count - 1)]
        down = [(j, i) for i, j in up]
        last = jnp.concatenate([lax.slice_in_dim(s, length - width, length, axis=dim) for s in shards])
        initial = jnp.concatenate([lax.slice_in_dim(s, 0, width, axis=dim) for s in shards])
        received.append((dim, lax.ppermute(last, axis, up), lax.ppermute(initial, axis, down)))
    done = []
    for (dim, before, after) in received:
        widths = [(0, 0)] * before.ndim
        for other, _, _ in done:
            widths[other] = (width, width)
        before, after = jnp.pad(before, widths), jnp.pad(after, widths)
        out = []
        offset = 0
        for s in shards:
            n = s.shape[0]
            out.append(jnp.concatenate([before[offset:offset + n], s, after[offset:offset + n]], axis=dim))
            offset += n
        shards = out
        done.append((dim, before, after))
    return shards


def neighbours(padded):
    middle = padded[..., 1:-1, 1:-1, :]
    zeros = jnp.zeros(middle.shape[:-1] + (1,), middle.dtype)
    return (
        padded[..., 2:, 1:-1, :],
        padded[..., :-2, 1:-1, :],
        padded[..., 1:-1, 2:, :],
        padded[..., 1:-1, :-2, :],
        jnp.concatenate([middle[..., 1:], zeros], axis=-1),
        jnp.concatenate([zeros, middle[..., :-1]], axis=-1),
    )


def apply(padded, faces, diagonal):
    field = padded[..., 1:-1, 1:-1, :]
    total = diagonal * field
    for weight, near in zip(faces, neighbours(padded)):
        total = total - weight * near
    return total


def gram(left, right):
    return jnp.einsum("axyz,bxyz->ab", left, right, precision=highest)


def combine(coef, field):
    return jnp.einsum("ab,axyz->bxyz", coef, field, precision=highest)


def solve_small(matrix, rhs):
    factor = jnp.linalg.cholesky(matrix)
    middle = lax.linalg.triangular_solve(factor, rhs, left_side=True, lower=True)
    return lax.linalg.triangular_solve(factor, middle, left_side=True, lower=True, transpose_a=True)


def extend(field):
    return with_halo([field], (("gx", 1), ("yz", 2)), 1)[0]


def combine_plane(coef, plane):
    return jnp.sum(coef[:, :, None, None, None] * plane[:, None], axis=0)


def planes_of(padded):
    return (padded[:, :1], padded[:, -1:], padded[:, :, :1], padded[:, :, -1:])


def add_planes(planes, coef, other):
    return tuple(p + combine_plane(coef, q) for p, q in zip(planes, other))


def padded_from(field, planes):
    x_before, x_after, y_before, y_after = planes
    wide = jnp.concatenate([x_before[:, :, 1:-1], field, x_after[:, :, 1:-1]], axis=1)
    return jnp.concatenate([y_before, wide, y_after], axis=2)


def shifted_sum(value, axis, stride, count):
    size = lax.axis_size(axis)
    total = value
    for step in range(1, count):
        pairs = [(i, (i + stride * step) % size) for i in range(size)]
        total = total + lax.ppermute(value, axis, pairs)
    return total


def reduce_grid(value):
    value = shifted_sum(value, "gx", 1, lax.axis_size("gx"))
    size = lax.axis_size("yz")
    value = value + lax.ppermute(value, "yz", [(i, i ^ 1) for i in range(size)])
    return shifted_sum(value, "yz", 2, size // 2)


def global_gram(left, right):
    return reduce_grid(gram(left, right))


def scatter_sources(partial_value):
    size = lax.axis_size("src")
    index = lax.axis_index("src")
    value = partial_value
    stride = size // 2
    while stride >= 1:
        width = value.shape[2] // 2
        keep = (index // stride) % 2
        mine = lax.dynamic_slice_in_dim(value, keep * width, width, axis=2)
        other = lax.dynamic_slice_in_dim(value, (1 - keep) * width, width, axis=2)
        value = mine + lax.ppermute(other, "src", [(i, i ^ stride) for i in range(size)])
        stride //= 2
    return value


def local_sources(count, cells, currents, electrodes, receivers, weights):
    size_x, size_y, size_z = cells
    lanes = 128 if size_z % 128 == 0 else size_z
    span_y = size_y * lax.axis_size("yz")
    anchor_x = lax.axis_index("gx") * size_x
    anchor_y = lax.axis_index("yz") * size_y
    columns = 2 * count
    total = columns * size_x * size_y * size_z

    def place(index, column):
        plane = span_y * size_z
        loc_x = index // plane - anchor_x
        loc_y = index % plane // size_z - anchor_y
        loc_z = index % size_z
        inside = (loc_x >= 0) & (loc_x < size_x) & (loc_y >= 0) & (loc_y < size_y)
        spot = (((loc_x * size_y + loc_y) * (size_z // lanes) + loc_z // lanes) * columns + column) * lanes + loc_z % lanes
        return jnp.where(inside, spot, total)

    local = jnp.arange(count, dtype=jnp.int32)
    spots = jnp.concatenate([
        place(electrodes[:, 0], local),
        place(electrodes[:, 1], local),
        place(receivers[None, :], count + local[:, None]).reshape(-1),
    ])
    values = jnp.concatenate([currents, -currents, weights.reshape(-1)])
    field = jnp.zeros((total,), jnp.float32).at[spots].add(values, mode="drop")
    field = field.reshape(size_x, size_y, size_z // lanes, columns, lanes)
    return jnp.transpose(field, (3, 0, 1, 2, 4)).reshape((columns,) + cells)


def on_device(warm_start, conductivity, currents, electrodes, receivers, weights):
    count = warm_start.shape[1]
    cells = warm_start.shape[2:]
    solution = warm_start.reshape((2 * count,) + cells)
    padded_cond, padded_solution = with_halo([conductivity[None], solution], (("gx", 1), ("yz", 2)), 1)
    padded_cond = padded_cond[0]
    faces = tuple((0.5 * (conductivity + near) for near in neighbours(padded_cond)))
    diagonal = faces[0]
    for weight in faces[1:]:
        diagonal = diagonal + weight
    rhs = local_sources(count, cells, currents, electrodes, receivers, weights)
    residual = rhs - apply(padded_solution, faces, diagonal)
    precond = residual / diagonal
    direction = precond
    inner = gram(residual, precond)
    padded_direction = extend(direction)
    image = apply(padded_direction, faces, diagonal)
    inner, curve = reduce_grid(jnp.stack([inner, gram(direction, image)]))
    solution_planes = planes_of(padded_solution)
    direction_planes = planes_of(padded_direction)
    alpha = solve_small(curve, inner)
    residual = residual - combine(alpha, image)
    precond = residual / diagonal
    padded_precond = extend(precond)
    precond_image = apply(padded_precond, faces, diagonal)
    fresh, self_curve, cross = reduce_grid(jnp.stack(
        [gram(residual, precond), gram(precond, precond_image), gram(precond, image)]))
    beta = solve_small(inner, fresh)
    mixed = jnp.matmul(cross, beta, precision=highest)
    curve = (self_curve + mixed + mixed.T
             + jnp.matmul(beta.T, jnp.matmul(curve, beta, precision=highest), precision=highest))
    last = solve_small(curve, fresh)
    first = alpha + jnp.matmul(beta, last, precision=highest)
    solution = solution + combine(first, direction) + combine(last, precond)
    solution_planes = add_planes(add_planes(solution_planes, first, direction_planes), last, planes_of(padded_precond))
    padded_solution = padded_from(solution, solution_planes)
    forward = solution[:count]
    adjoint = solution[count:]
    total = jnp.zeros(cells, jnp.float32)
    for near_fwd, near_adj in zip(
        neighbours(padded_solution[:count]), neighbours(padded_solution[count:])
    ):
        total = total + jnp.sum((forward - near_fwd) * (adjoint - near_adj), axis=0)
    partial_value = -0.5 * total
    gradient = scatter_sources(partial_value)
    return (solution.reshape(warm_start.shape), gradient)


def solution(mesh):
    return jax.shard_map(
        on_device,
        mesh=mesh,
        in_specs=(
            P(None, "src", "gx", "yz", None),
            P("gx", "yz", None),
            P("src"),
            P("src", None),
            P(),
            P("src", None),
        ),
        out_specs=(P(None, "src", "gx", "yz", None), P("gx", "yz", "src")),
        check_vma=False,
    )
```
